128 devices in a mesh: body: 4 (over x), dom: 32 (over y, z, core).
Axes of the slice: x: 4, y: 4, z: 4, core: 2. Of those that a mesh axis runs over, the one named last changes fastest.
Arguments:
- master_basis: bfloat16 [65536, 16, 256], P(('body', 'dom')), may hold values from -1.5 to 1.5
- master_weights: bfloat16 [65536, 4, 16], P(('body', 'dom')), may hold values from 0.099609375 to 1
- master_dest: int32 [65536, 1], P(('body', 'dom')), may hold values from 0 to 31; in each aligned block of 512 rows (0 to 511, 512 to 1023, ...) at most 32 rows name the same one
- master_slaves: int32 [65536, 4], P(('body', 'dom')), may hold values from 0 to 511
- slave_basis: bfloat16 [65536, 16, 256], P(('body', 'dom')), may hold values from -1.5 to 1.5
- slave_gain: float32 [65536], P(('body', 'dom')), may hold values from 0.1 to 1
- tile_owner: int32 [4096, 1], P(('body', 'dom')), may hold values from 0 to 31; in each aligned block of 32 rows (0 to 31, 32 to 63, ...) at most 2 rows name the same one
- tile_row: int32 [4096], P(('body', 'dom')), may hold values from 0 to 15
Outputs:
- coupling: float32 [2048, 256, 256], P(('body', 'dom'))
The draws below stay inside these ranges and needn't reach their ends.
Inputs may be any that keep to these rules, and one draw needn't show every extreme that they name: `master_dest`: among the master segments of one device at most 32 name the same dom index, and that many is reached. `tile_owner`: among the tiles of one device at most 2 name the same owner, and that many is reached.
All inputs are finite; a program needn't handle non-finite values.
Results may differ from the reference program's by a relative error of at most 0.0027.
Values may be sent and summed in bfloat16 or wider, within the bound.
No kernel may reach another device: no remote copies, remote signals or barrier semaphores. Data moves between devices by JAX's collectives and lax.ppermute only.
A program may use at most 256 MiB of HBM per device.

```python
import math
import jax
import jax.numpy as jnp
import numpy as np
from jax import lax

NP = 256
Q = 16
PAIRS = 4
SEG_DEV = 512
SLV_DEV = 512
TILE_DEV = 32
BR = 16
CAP = 32
TCAP = 2
SEGS = 65536
SLAVES = 65536
TILES = 4096
ROWS = 2048
N_BODY = 4
N_DOM = 32


def place_ends(array, key, low, high):
    longest = array.shape.index(max(array.shape))
    spots = []
    for shift in (0, 1):
        where = [jax.random.randint(jax.random.fold_in(key, axis), (), 0, length) for axis, length in enumerate(array.shape)]
        where[longest] = (where[longest] + shift) % array.shape[longest]
        spots.append(tuple(where))
    return array.at[spots[0]].set(low).at[spots[1]].set(high)


def level_of(stream_key, extent, shards, least, top_value):
    loudness, own = 1.0, jax.random.fold_in(stream_key, 6)
    for dim, parts in shards:
        draws = jnp.exp(jax.random.uniform(jax.random.fold_in(own, dim), (parts,), jnp.float32, least / len(shards), top_value / len(shards)))
        loudness = loudness * jnp.repeat(draws, extent[dim] // parts).reshape([-1 if axis == dim else 1 for axis in range(len(extent))])
    return loudness


def deal_out(stream_key, own, number, rows, amount, top, bound, lean):
    order = jax.random.permutation(stream_key, amount)
    heavy_load, common = load_shares(amount, rows * top, bound, lean, True), load_shares(amount, rows * top, bound, lean, False)
    places = jnp.arange(amount)

    def named(tallies, rotation):
        used = int((tallies > 0).sum())
        fixed = max(1, used // 4)
        moved = fixed + (places - fixed + rotation * (used - fixed)) % max(1, amount - fixed)
        return jnp.zeros((amount,), jnp.int32).at[order[jnp.where(places < fixed, places, moved)]].set(jnp.asarray(tallies, jnp.int32))

    tallies = jnp.where(number % 4 == 0, named(heavy_load, number // 4), named(common, number - number // 4 - 1))
    mixed = jax.random.permutation(jax.random.fold_in(own, 3), amount)
    source_of, taker = mixed[0:amount // 2 * 2:2], mixed[1:amount // 2 * 2:2]
    margin = jnp.minimum(tallies[source_of] - 1, bound - tallies[taker]) // 2
    margin = jnp.where((source_of == order[0]) | (taker == order[0]) | (tallies[taker] == 0), 0, jnp.maximum(margin, 0))
    moved = jax.random.randint(jax.random.fold_in(own, 4), (amount // 2,), 0, 1 << 20) % (margin + 1)
    tallies = tallies.at[source_of].add(-moved).at[taker].add(moved)
    items = jnp.searchsorted(jnp.cumsum(tallies), jnp.arange(rows * top), side="right").astype(jnp.int32)
    grid = items.reshape(top, rows).T
    grid = grid[jax.random.permutation(jax.random.fold_in(own, 1), rows)]
    rotation = jax.random.randint(jax.random.fold_in(own, 2), (rows, 1), 0, top)
    return jnp.take_along_axis(grid, (jnp.arange(top)[None, :] + rotation) % top, axis=1)


def load_shares(number_of, total, bound, skew, full):
    loads = [(1 << 20) // math.isqrt(rank ** skew) + 1 for rank in range(1, number_of + 1)]
    largest = bound if full else min(bound, max(-(-total // number_of), total * loads[0] // sum(loads)))
    least = 1 if total - largest >= number_of - 1 else 0
    holding, rest = [largest] + [least] * (number_of - 1), total - largest - least * (number_of - 1)
    while rest > 0:
        candidates = [i for i in range(1, number_of) if holding[i] < largest] or [i for i in range(1, number_of) if holding[i] < bound]
        mass, left = sum([loads[i] for i in candidates]), rest
        for i in candidates:
            more = min(bound - holding[i], max(1, left * loads[i] // mass), rest)
            holding[i] = holding[i] + more
            rest = rest - more
    return np.array(holding)


def noise(key, extent, width, limit, cuts=(), held_as=jnp.bfloat16):
    drawn = jax.random.normal(key, extent, jnp.float32) * width
    if len(cuts) > 0:
        drawn = level_of(key, extent, cuts, -0.22, 0.18) * drawn
    return jnp.clip(drawn, min=-limit, max=limit).astype(held_as)


def setup_inputs(seed: int = 0) -> dict:
    splits = jax.random.split(jax.random.key(seed), 9)
    master_basis = noise(splits[0], (SEGS, Q, NP), 0.25, 1.5, ((0, 128),))
    master_weights = jnp.clip(jnp.exp(math.log(1.0) - 2.306499 * jax.random.uniform(splits[1], (SEGS, PAIRS, Q), jnp.float32) ** level_of(splits[1], (SEGS, PAIRS, Q), ((0, 128),), -0.2, 0.2)), 0.099609375, 1.0).astype(jnp.bfloat16)
    master_dest_keys = jax.random.split(jax.random.fold_in(splits[2], 1), SEGS // SEG_DEV)
    master_dest_turns = jax.random.permutation(jax.random.fold_in(splits[2], 3), SEGS // SEG_DEV)
    master_dest = jax.vmap(lambda own, number: deal_out(jax.random.fold_in(splits[2], 2), own, number, SEG_DEV, N_DOM, 1, CAP, 2))(master_dest_keys, master_dest_turns).reshape((SEGS, 1))
    master_slaves = place_ends(jax.random.randint(splits[3], (SEGS, PAIRS), 0, SLV_DEV), jax.random.fold_in(splits[3], 1), 0, SLV_DEV - 1).astype(jnp.int32)
    slave_basis = noise(splits[4], (SLAVES, Q, NP), 0.25, 1.5, ((0, 128),))
    slave_gain = jnp.clip(jnp.exp(math.log(1.0) - 2.3025851 * jax.random.uniform(splits[5], (SLAVES,), jnp.float32) ** level_of(splits[5], (SLAVES,), ((0, 128),), -0.2, 0.2)), 0.1, 1.0)
    tile_owner_keys = jax.random.split(jax.random.fold_in(splits[6], 1), TILES // TILE_DEV)
    tile_owner_turns = jax.random.permutation(jax.random.fold_in(splits[6], 3), TILES // TILE_DEV)
    tile_owner = jax.vmap(lambda own, number: deal_out(jax.random.fold_in(splits[6], 2), own, number, TILE_DEV, N_DOM, 1, TCAP, 2))(tile_owner_keys, tile_owner_turns).reshape((TILES, 1))
    tile_row = place_ends(jax.random.randint(splits[7], (TILES,), 0, BR), jax.random.fold_in(splits[7], 1), 0, BR - 1).astype(jnp.int32)
    return {"master_basis": master_basis, "master_weights": master_weights, "master_dest": master_dest, "master_slaves": master_slaves, "slave_basis": slave_basis, "slave_gain": slave_gain, "tile_owner": tile_owner, "tile_row": tile_row}


def reference(master_basis, master_weights, master_dest, master_slaves, slave_basis, slave_gain, tile_owner, tile_row):
    body_count = N_BODY
    dom_count = N_DOM
    source_dev = (jnp.arange(SEGS, dtype=jnp.int32) // SEG_DEV).astype(jnp.int32)
    target_dev = ((source_dev // dom_count + 1) % body_count) * dom_count + master_dest[:, 0]
    slave_global = (target_dev[:, None] * SLV_DEV + master_slaves).astype(jnp.int32)

    def add_block(block, carry):
        far_sum, weight_sum = carry
        first_row = (block * SEG_DEV).astype(jnp.int32)
        basis_rows = lax.dynamic_slice_in_dim(master_basis, first_row, SEG_DEV, 0).astype(jnp.float32)
        weights = lax.dynamic_slice_in_dim(master_weights, first_row, SEG_DEV, 0).astype(jnp.float32)
        slot_index = lax.dynamic_slice_in_dim(slave_global, first_row, SEG_DEV, 0).reshape(-1)
        weighted = weights[:, :, :, None] * basis_rows[:, None, :, :]
        far_sum = far_sum.at[slot_index].add(weighted.reshape(-1, Q, NP))
        weight_sum = weight_sum.at[slot_index].add(weights.reshape(-1, Q))
        return far_sum, weight_sum

    far_sum = jnp.zeros((SLAVES, Q, NP), jnp.float32)
    weight_sum = jnp.zeros((SLAVES, Q), jnp.float32)
    far_sum, weight_sum = lax.fori_loop(0, body_count * dom_count, add_block, (far_sum, weight_sum))
    slave_values = slave_basis.astype(jnp.float32)
    flux = ((slave_gain[:, None] + weight_sum)[:, :, None] * slave_values - far_sum).astype(jnp.bfloat16)
    per_tile = SLV_DEV // TILE_DEV
    left = slave_values.reshape(TILES, per_tile * Q, NP)
    right = flux.astype(jnp.float32).reshape(TILES, per_tile * Q, NP)
    coupling_tiles = jnp.einsum("tkn,tkm->tnm", left, right).astype(jnp.bfloat16)
    tile_dev = (jnp.arange(TILES, dtype=jnp.int32) // TILE_DEV).astype(jnp.int32)
    dest_row = ((tile_dev // dom_count) * dom_count + tile_owner[:, 0]) * BR + tile_row
    coupling = jnp.zeros((ROWS, NP, NP), jnp.float32).at[dest_row].add(coupling_tiles.astype(jnp.float32))
    return coupling
```

```python
import jax
import jax.numpy as jnp
from jax import lax
from jax.sharding import PartitionSpec as P

NP = 256
Q = 16
PAIRS = 4
BR = 16
SPLIT = 2


def shifted(block, axis, distance):
    devices = range(lax.axis_size(axis))
    route = [((i - distance) % len(devices), i) for i in devices]
    return lax.ppermute(block, axis, route)


def slot_of(target, groups, capacity):
    onehot = (target[:, None] == jnp.arange(groups, dtype=jnp.int32)[None, :]).astype(jnp.int32)
    before = jnp.cumsum(onehot, axis=0) - onehot
    position = jnp.sum(before * onehot, axis=1)
    return target * capacity + position


def placer_of(slot, slots):
    return slot[None, :] == jnp.arange(slots, dtype=jnp.int32)[:, None]


def on_device(
    master_basis,
    master_weights,
    master_dest,
    master_slaves,
    slave_basis,
    slave_gain,
    tile_owner,
    tile_row,
):
    f32, bf16, i32 = jnp.float32, jnp.bfloat16, jnp.int32
    dom_count = lax.axis_size("dom")
    seg_count = master_basis.shape[0]
    capacity = 2 * seg_count // dom_count
    slots = dom_count * capacity
    slave_count = slave_basis.shape[0]
    tile_count = tile_row.shape[0]
    per_tile = slave_count // tile_count
    tile_capacity = max(2, 2 * tile_count // dom_count)
    tile_slots = dom_count * tile_capacity
    width = NP // SPLIT
    wcols = PAIRS * Q

    meta = jnp.concatenate(
        [
            master_weights.reshape(seg_count, wcols).astype(f32),
            master_dest.astype(f32),
            master_slaves.astype(f32) + 1.0,
        ],
        axis=1,
    )
    moved_meta = shifted(meta, "body", 1)
    moved_chunks = []
    for k in range(SPLIT):
        piece = master_basis[:, :, k * width:(k + 1) * width]
        if moved_chunks:
            piece, _ = lax.optimization_barrier((piece, moved_chunks[-1]))
        moved_chunks.append(shifted(piece, "body", 1))

    moved_dest = moved_meta[:, wcols].astype(i32)
    slot = slot_of(moved_dest, dom_count, capacity)
    placer = placer_of(slot, slots)
    records = jnp.concatenate([moved_meta[:, :wcols], moved_meta[:, wcols + 1:]], axis=1)
    packed_meta = jnp.dot(placer.astype(f32), records, precision=lax.Precision.HIGHEST)
    rec_cols = records.shape[1]

    tile_slot = slot_of(tile_owner[:, 0], dom_count, tile_capacity)
    tile_placer = placer_of(tile_slot, tile_slots)
    packed_rows = jnp.dot(tile_placer.astype(i32), tile_row + 1).astype(f32)

    send_meta = jnp.concatenate(
        [
            packed_meta.reshape(dom_count, capacity * rec_cols),
            packed_rows.reshape(dom_count, tile_capacity),
        ],
        axis=1,
    )
    got_meta = lax.all_to_all(send_meta, "dom", 0, 0, tiled=True)

    got_chunks = []
    for k in range(SPLIT):
        packed = jnp.dot(
            placer.astype(bf16),
            moved_chunks[k].reshape(seg_count, Q * width),
            preferred_element_type=f32,
        ).astype(bf16)
        got_chunks.append(
            lax.all_to_all(packed.reshape(dom_count, capacity, Q * width), "dom", 0, 0, tiled=True)
        )

    got_records = got_meta[:, : capacity * rec_cols].reshape(slots, rec_cols)
    got_weights = got_records[:, :wcols].reshape(slots, PAIRS, Q)
    got_owners = got_records[:, wcols:].astype(i32) - 1
    slave_ids = jnp.arange(slave_count, dtype=i32)
    table = None
    for p in range(PAIRS):
        term = jnp.where(
            got_owners[None, None, :, p] == slave_ids[None, :, None],
            jnp.transpose(got_weights[:, p, :])[:, None, :],
            0.0,
        )
        table = term if table is None else table + term
    table_hi = table.astype(bf16)
    table_lo = (table - table_hi.astype(f32)).astype(bf16)
    weight_sum = jnp.transpose(jnp.sum(table, axis=2))
    scale = (slave_gain[:, None] + weight_sum)[:, :, None]

    got_rows = got_meta[:, capacity * rec_cols:].reshape(tile_slots).astype(i32) - 1
    selector = (got_rows[None, :] == jnp.arange(BR, dtype=i32)[:, None]).astype(bf16)
    left = slave_basis.reshape(tile_count, per_tile * Q, NP)

    parts = []
    for k in range(SPLIT):
        rows = got_chunks[k].reshape(slots, Q, width)
        far_sum = jnp.einsum("qsr,rqn->sqn", table_hi, rows, preferred_element_type=f32)
        far_sum = far_sum + jnp.einsum("qsr,rqn->sqn", table_lo, rows, preferred_element_type=f32)
        own = slave_basis[:, :, k * width:(k + 1) * width].astype(f32)
        flux = (scale * own - far_sum).astype(bf16)
        tiles = jnp.einsum(
            "tkn,tkm->tnm",
            left,
            flux.reshape(tile_count, per_tile * Q, width),
            preferred_element_type=f32,
        ).astype(bf16)
        packed_tiles = jnp.dot(
            tile_placer.astype(bf16),
            tiles.reshape(tile_count, NP * width),
            preferred_element_type=f32,
        ).astype(bf16)
        got_tiles = lax.all_to_all(
            packed_tiles.reshape(dom_count, tile_capacity * NP, width), "dom", 0, 0, tiled=True
        )
        part = jnp.dot(
            selector,
            got_tiles.reshape(tile_slots, NP * width),
            preferred_element_type=f32,
        )
        parts.append(part.reshape(BR, NP, width))
    return jnp.concatenate(parts, axis=2)


def solution(mesh):
    return jax.shard_map(
        on_device,
        mesh=mesh,
        in_specs=(
            P(("body", "dom"), None, None),
            P(("body", "dom"), None, None),
            P(("body", "dom"), None),
            P(("body", "dom"), None),
            P(("body", "dom"), None, None),
            P(("body", "dom")),
            P(("body", "dom"), None),
            P(("body", "dom")),
        ),
        out_specs=P(("body", "dom"), None, None),
        check_vma=False,
    )
```

```python
import functools

import jax
import jax.numpy as jnp
from jax import lax
from jax.experimental import pallas as pl
from jax.experimental.pallas import tpu as pltpu
from jax.sharding import PartitionSpec as P

NP = 256
Q = 16
PAIRS = 4
BR = 16
SPLIT = 2


def shifted(block, axis, distance):
    devices = range(lax.axis_size(axis))
    route = [((i - distance) % len(devices), i) for i in devices]
    return lax.ppermute(block, axis, route)


def slot_of(target, groups, capacity):
    onehot = (target[:, None] == jnp.arange(groups, dtype=jnp.int32)[None, :]).astype(jnp.int32)
    before = jnp.cumsum(onehot, axis=0) - onehot
    position = jnp.sum(before * onehot, axis=1)
    return target * capacity + position


def placer_of(slot, slots):
    return slot[None, :] == jnp.arange(slots, dtype=jnp.int32)[:, None]


def flux_kernel(hi_ref, lo_ref, rows_ref, own_ref, scale_ref, out_ref):
    rows = rows_ref[...]
    far = jnp.dot(hi_ref[0], rows, preferred_element_type=jnp.float32)
    far = far + jnp.dot(lo_ref[0], rows, preferred_element_type=jnp.float32)
    out_ref[0] = (scale_ref[0] * own_ref[0].astype(jnp.float32) - far).astype(jnp.bfloat16)


def flux_chunk(table_hi, table_lo, rows, own, scale, chunk):
    q_count, slave_count, slots = table_hi.shape
    width = rows.shape[1] // q_count
    return pl.pallas_call(
        flux_kernel,
        grid=(q_count,),
        in_specs=[
            pl.BlockSpec((1, slave_count, slots), lambda q: (q, 0, 0)),
            pl.BlockSpec((1, slave_count, slots), lambda q: (q, 0, 0)),
            pl.BlockSpec((slots, width), lambda q: (0, q)),
            pl.BlockSpec((1, slave_count, width), lambda q: (q, 0, chunk)),
            pl.BlockSpec((1, slave_count, 1), lambda q: (q, 0, 0)),
        ],
        out_specs=pl.BlockSpec((1, slave_count, width), lambda q: (q, 0, 0)),
        out_shape=jax.ShapeDtypeStruct((q_count, slave_count, width), jnp.bfloat16),
    )(table_hi, table_lo, rows, own, scale)


def tile_kernel(tile_count, source_ref, left_ref, flux_ref, out_ref):
    x = pl.program_id(0)
    real = source_ref[x] < tile_count

    @pl.when(real)
    def _():
        q_count, per_tile, width = flux_ref.shape
        right = flux_ref[...].reshape(q_count * per_tile, width)
        out_ref[0] = jnp.dot(left_ref[0], right, preferred_element_type=jnp.float32).astype(jnp.bfloat16)

    @pl.when(jnp.logical_not(real))
    def _():
        out_ref[...] = jnp.zeros(out_ref.shape, out_ref.dtype)


def packed_tiles_of(source, left, flux, per_tile):
    tile_slots = source.shape[0]
    tile_count, rows, depth = left.shape
    q_count, slave_count, width = flux.shape
    last = tile_count - 1
    grid_spec = pltpu.PrefetchScalarGridSpec(
        num_scalar_prefetch=1,
        grid=(tile_slots,),
        in_specs=[
            pl.BlockSpec((1, rows, depth), lambda x, src: (jnp.minimum(src[x], last), 0, 0)),
            pl.BlockSpec((q_count, per_tile, width), lambda x, src: (0, jnp.minimum(src[x], last), 0)),
        ],
        out_specs=pl.BlockSpec((1, rows, width), lambda x, src: (x, 0, 0)),
    )
    return pl.pallas_call(
        functools.partial(tile_kernel, tile_count),
        grid_spec=grid_spec,
        out_shape=jax.ShapeDtypeStruct((tile_slots, rows, width), jnp.bfloat16),
    )(source, left, flux)


def on_device(
    master_basis,
    master_weights,
    master_dest,
    master_slaves,
    slave_basis,
    slave_gain,
    tile_owner,
    tile_row,
):
    f32, bf16, i32 = jnp.float32, jnp.bfloat16, jnp.int32
    dom_count = lax.axis_size("dom")
    seg_count = master_basis.shape[0]
    capacity = 2 * seg_count // dom_count
    slots = dom_count * capacity
    slave_count = slave_basis.shape[0]
    tile_count = tile_row.shape[0]
    per_tile = slave_count // tile_count
    tile_capacity = max(2, 2 * tile_count // dom_count)
    tile_slots = dom_count * tile_capacity
    width = NP // SPLIT
    wcols = PAIRS * Q

    meta = jnp.concatenate(
        [
            master_weights.reshape(seg_count, wcols).astype(f32),
            master_dest.astype(f32),
            master_slaves.astype(f32) + 1.0,
        ],
        axis=1,
    )
    moved_meta = shifted(meta, "body", 1)
    moved_chunks = []
    for k in range(SPLIT):
        piece = master_basis[:, :, k * width:(k + 1) * width]
        if moved_chunks:
            piece, _ = lax.optimization_barrier((piece, moved_chunks[-1]))
        moved_chunks.append(shifted(piece, "body", 1))

    moved_dest = moved_meta[:, wcols].astype(i32)
    slot = slot_of(moved_dest, dom_count, capacity)
    placer = placer_of(slot, slots)
    records = jnp.concatenate([moved_meta[:, :wcols], moved_meta[:, wcols + 1:]], axis=1)
    packed_meta = jnp.dot(placer.astype(f32), records, precision=lax.Precision.HIGHEST)
    rec_cols = records.shape[1]

    tile_slot = slot_of(tile_owner[:, 0], dom_count, tile_capacity)
    tile_placer = placer_of(tile_slot, tile_slots)
    packed_rows = jnp.dot(tile_placer.astype(i32), tile_row + 1).astype(f32)

    send_meta = jnp.concatenate(
        [
            packed_meta.reshape(dom_count, capacity * rec_cols),
            packed_rows.reshape(dom_count, tile_capacity),
        ],
        axis=1,
    )
    got_meta = lax.all_to_all(send_meta, "dom", 0, 0, tiled=True)

    got_chunks = []
    for k in range(SPLIT):
        packed = jnp.dot(
            placer.astype(bf16),
            moved_chunks[k].reshape(seg_count, Q * width),
            preferred_element_type=f32,
        ).astype(bf16)
        got_chunks.append(
            lax.all_to_all(packed.reshape(dom_count, capacity, Q * width), "dom", 0, 0, tiled=True)
        )

    got_records = got_meta[:, : capacity * rec_cols].reshape(slots, rec_cols)
    got_weights = got_records[:, :wcols].reshape(slots, PAIRS, Q)
    got_owners = got_records[:, wcols:].astype(i32) - 1
    slave_ids = jnp.arange(slave_count, dtype=i32)
    table = None
    for p in range(PAIRS):
        term = jnp.where(
            got_owners[None, None, :, p] == slave_ids[None, :, None],
            jnp.transpose(got_weights[:, p, :])[:, None, :],
            0.0,
        )
        table = term if table is None else table + term
    table_hi = table.astype(bf16)
    table_lo = (table - table_hi.astype(f32)).astype(bf16)
    weight_sum = jnp.sum(table, axis=2)
    table_hi, table_lo, weight_sum = lax.optimization_barrier((table_hi, table_lo, weight_sum))
    scale = (jnp.transpose(slave_gain[:, None]) + weight_sum)[:, :, None]

    got_rows = got_meta[:, capacity * rec_cols:].reshape(tile_slots).astype(i32) - 1
    selector = (got_rows[None, :] == jnp.arange(BR, dtype=i32)[:, None]).astype(bf16)
    tile_source = jnp.dot(tile_placer.astype(i32), jnp.arange(1, tile_count + 1, dtype=i32)) - 1
    tile_source = jnp.where(tile_source < 0, tile_count, tile_source)
    own = jnp.transpose(slave_basis, (1, 0, 2))
    left = jnp.transpose(
        slave_basis.reshape(tile_count, per_tile, Q, NP), (0, 3, 2, 1)
    ).reshape(tile_count, NP, Q * per_tile)

    parts = []
    for k in range(SPLIT):
        rows = got_chunks[k].reshape(slots, Q * width)
        flux = flux_chunk(table_hi, table_lo, rows, own, scale, k)
        packed_tiles = packed_tiles_of(tile_source, left, flux, per_tile)
        got_tiles = lax.all_to_all(
            packed_tiles.reshape(dom_count, tile_capacity * NP, width), "dom", 0, 0, tiled=True
        )
        part = jnp.einsum(
            "bx,xnm->bnm",
            selector,
            got_tiles.reshape(tile_slots, NP, width),
            preferred_element_type=f32,
        )
        parts.append(part)
    return jnp.concatenate(parts, axis=2)


def solution(mesh):
    return jax.shard_map(
        on_device,
        mesh=mesh,
        in_specs=(
            P(("body", "dom"), None, None),
            P(("body", "dom"), None, None),
            P(("body", "dom"), None),
            P(("body", "dom"), None),
            P(("body", "dom"), None, None),
            P(("body", "dom")),
            P(("body", "dom"), None),
            P(("body", "dom")),
        ),
        out_specs=P(("body", "dom"), None, None),
        check_vma=False,
    )
```

```python
import functools

import jax
import jax.numpy as jnp
from jax import lax
from jax.experimental import pallas as pl
from jax.experimental.pallas import tpu as pltpu
from jax.sharding import PartitionSpec as P

NP = 256
Q = 16
PAIRS = 4
BR = 16
SPLIT = 2


def shifted(block, axis, distance):
    devices = range(lax.axis_size(axis))
    route = [((i - distance) % len(devices), i) for i in devices]
    return lax.ppermute(block, axis, route)


def slot_of(target, groups, capacity):
    onehot = (target[:, None] == jnp.arange(groups, dtype=jnp.int32)[None, :]).astype(jnp.int32)
    before = jnp.cumsum(onehot, axis=0) - onehot
    position = jnp.sum(before * onehot, axis=1)
    return target * capacity + position


def placer_of(slot, slots):
    return slot[None, :] == jnp.arange(slots, dtype=jnp.int32)[:, None]


def flux_kernel(hi_ref, lo_ref, rows_ref, own_ref, scale_ref, out_ref):
    rows = rows_ref[...]
    far = jnp.dot(hi_ref[0], rows, preferred_element_type=jnp.float32)
    far = far + jnp.dot(lo_ref[0], rows, preferred_element_type=jnp.float32)
    out_ref[0] = (scale_ref[0] * own_ref[0].astype(jnp.float32) - far).astype(jnp.bfloat16)


def flux_chunk(table_hi, table_lo, rows, own, scale, chunk):
    q_count, slave_count, slots = table_hi.shape
    width = rows.shape[1] // q_count
    return pl.pallas_call(
        flux_kernel,
        grid=(q_count,),
        in_specs=[
            pl.BlockSpec((1, slave_count, slots), lambda q: (q, 0, 0)),
            pl.BlockSpec((1, slave_count, slots), lambda q: (q, 0, 0)),
            pl.BlockSpec((slots, width), lambda q: (0, q)),
            pl.BlockSpec((1, slave_count, width), lambda q: (q, 0, chunk)),
            pl.BlockSpec((1, slave_count, 1), lambda q: (q, 0, 0)),
        ],
        out_specs=pl.BlockSpec((1, slave_count, width), lambda q: (q, 0, 0)),
        out_shape=jax.ShapeDtypeStruct((q_count, slave_count, width), jnp.bfloat16),
    )(table_hi, table_lo, rows, own, scale)


def tile_kernel(tile_count, per_tile, source_ref, left_ref, flux_ref, out_ref):
    width = out_ref.shape[2]

    def body(x, carry):
        src = source_ref[x]

        @pl.when(src < tile_count)
        def _():
            first = pl.multiple_of(src * per_tile, per_tile)
            right = flux_ref[:, pl.ds(first, per_tile), :].reshape(-1, width)
            out_ref[x] = jnp.dot(
                left_ref[src], right, preferred_element_type=jnp.float32
            ).astype(jnp.bfloat16)

        @pl.when(src >= tile_count)
        def _():
            out_ref[x] = jnp.zeros(out_ref.shape[1:], out_ref.dtype)

        return carry

    lax.fori_loop(0, out_ref.shape[0], body, 0)


def packed_tiles_of(source, left, flux, per_tile):
    tile_slots = source.shape[0]
    tile_count, rows, depth = left.shape
    width = flux.shape[2]
    vmem = pltpu.MemorySpace.VMEM if hasattr(pltpu, "MemorySpace") else pltpu.TPUMemorySpace.VMEM
    return pl.pallas_call(
        functools.partial(tile_kernel, tile_count, per_tile),
        in_specs=[
            pl.BlockSpec(memory_space=pltpu.SMEM),
            pl.BlockSpec(memory_space=vmem),
            pl.BlockSpec(memory_space=vmem),
        ],
        out_specs=pl.BlockSpec(memory_space=vmem),
        out_shape=jax.ShapeDtypeStruct((tile_slots, rows, width), jnp.bfloat16),
    )(source, left, flux)


def on_device(
    master_basis,
    master_weights,
    master_dest,
    master_slaves,
    slave_basis,
    slave_gain,
    tile_owner,
    tile_row,
):
    f32, bf16, i32 = jnp.float32, jnp.bfloat16, jnp.int32
    dom_count = lax.axis_size("dom")
    seg_count = master_basis.shape[0]
    capacity = 2 * seg_count // dom_count
    slots = dom_count * capacity
    slave_count = slave_basis.shape[0]
    tile_count = tile_row.shape[0]
    per_tile = slave_count // tile_count
    tile_capacity = max(2, 2 * tile_count // dom_count)
    tile_slots = dom_count * tile_capacity
    width = NP // SPLIT
    wcols = PAIRS * Q

    meta = jnp.concatenate(
        [
            master_weights.reshape(seg_count, wcols).astype(f32),
            master_dest.astype(f32),
            master_slaves.astype(f32) + 1.0,
        ],
        axis=1,
    )
    moved_meta = shifted(meta, "body", 1)
    moved_chunks = []
    for k in range(SPLIT):
        piece = master_basis[:, :, k * width:(k + 1) * width]
        if moved_chunks:
            piece, _ = lax.optimization_barrier((piece, moved_chunks[-1]))
        moved_chunks.append(shifted(piece, "body", 1))

    moved_dest = moved_meta[:, wcols].astype(i32)
    slot = slot_of(moved_dest, dom_count, capacity)
    placer = placer_of(slot, slots)
    records = jnp.concatenate([moved_meta[:, :wcols], moved_meta[:, wcols + 1:]], axis=1)
    packed_meta = jnp.dot(placer.astype(f32), records, precision=lax.Precision.HIGHEST)
    rec_cols = records.shape[1]

    tile_slot = slot_of(tile_owner[:, 0], dom_count, tile_capacity)
    tile_placer = placer_of(tile_slot, tile_slots)
    packed_rows = jnp.dot(tile_placer.astype(i32), tile_row + 1).astype(f32)

    send_meta = jnp.concatenate(
        [
            packed_meta.reshape(dom_count, capacity * rec_cols),
            packed_rows.reshape(dom_count, tile_capacity),
        ],
        axis=1,
    )
    got_meta = lax.all_to_all(send_meta, "dom", 0, 0, tiled=True)

    got_records = got_meta[:, : capacity * rec_cols].reshape(slots, rec_cols)
    got_weights = got_records[:, :wcols].reshape(slots, PAIRS, Q)
    got_owners = got_records[:, wcols:].astype(i32) - 1
    slave_ids = jnp.arange(slave_count, dtype=i32)
    table = None
    for p in range(PAIRS):
        term = jnp.where(
            got_owners[None, None, :, p] == slave_ids[None, :, None],
            jnp.transpose(got_weights[:, p, :])[:, None, :],
            0.0,
        )
        table = term if table is None else table + term
    table_hi = table.astype(bf16)
    table_lo = (table - table_hi.astype(f32)).astype(bf16)
    weight_sum = jnp.sum(table, axis=2)
    tables = lax.optimization_barrier((table_hi, table_lo, weight_sum))
    table_hi, table_lo, weight_sum = tables
    scale = (jnp.transpose(slave_gain[:, None]) + weight_sum)[:, :, None]

    got_chunks = []
    for k in range(SPLIT):
        moved = moved_chunks[k]
        if k == 1:
            moved, _ = lax.optimization_barrier((moved, tables))
        packed = jnp.dot(
            placer.astype(bf16),
            moved.reshape(seg_count, Q * width),
            preferred_element_type=f32,
        ).astype(bf16)
        got_chunks.append(
            lax.all_to_all(packed.reshape(dom_count, capacity, Q * width), "dom", 0, 0, tiled=True)
        )

    got_rows = got_meta[:, capacity * rec_cols:].reshape(tile_slots).astype(i32) - 1
    selector = (got_rows[None, :] == jnp.arange(BR, dtype=i32)[:, None]).astype(bf16)
    tile_source = jnp.dot(tile_placer.astype(i32), jnp.arange(1, tile_count + 1, dtype=i32)) - 1
    tile_source = jnp.where(tile_source < 0, tile_count, tile_source)
    own = jnp.transpose(slave_basis, (1, 0, 2))
    left = jnp.transpose(
        slave_basis.reshape(tile_count, per_tile, Q, NP), (0, 3, 2, 1)
    ).reshape(tile_count, NP, Q * per_tile)

    parts = []
    for k in range(SPLIT):
        rows = got_chunks[k].reshape(slots, Q * width)
        flux = flux_chunk(table_hi, table_lo, rows, own, scale, k)
        packed_tiles = packed_tiles_of(tile_source, left, flux, per_tile)
        got_tiles = lax.all_to_all(
            packed_tiles.reshape(dom_count, tile_capacity * NP, width), "dom", 0, 0, tiled=True
        )
        part = jnp.einsum(
            "bx,xnm->bnm",
            selector,
            got_tiles.reshape(tile_slots, NP, width),
            preferred_element_type=f32,
        )
        parts.append(part)
    return jnp.concatenate(parts, axis=2)


def solution(mesh):
    return jax.shard_map(
        on_device,
        mesh=mesh,
        in_specs=(
            P(("body", "dom"), None, None),
            P(("body", "dom"), None, None),
            P(("body", "dom"), None),
            P(("body", "dom"), None),
            P(("body", "dom"), None, None),
            P(("body", "dom")),
            P(("body", "dom"), None),
            P(("body", "dom")),
        ),
        out_specs=P(("body", "dom"), None, None),
        check_vma=False,
    )
```

```python
import functools

import jax
import jax.numpy as jnp
from jax import lax
from jax.experimental import pallas as pl
from jax.experimental.pallas import tpu as pltpu
from jax.sharding import PartitionSpec as P

NP = 256
Q = 16
PAIRS = 4
BR = 16
SPLIT = 2


def shifted(block, axis, distance):
    devices = range(lax.axis_size(axis))
    route = [((i - distance) % len(devices), i) for i in devices]
    return lax.ppermute(block, axis, route)


def slot_of(target, groups, capacity):
    onehot = (target[:, None] == jnp.arange(groups, dtype=jnp.int32)[None, :]).astype(jnp.int32)
    before = jnp.cumsum(onehot, axis=0) - onehot
    position = jnp.sum(before * onehot, axis=1)
    return target * capacity + position


def placer_of(slot, slots):
    return slot[None, :] == jnp.arange(slots, dtype=jnp.int32)[:, None]


def flux_kernel(hi_ref, lo_ref, rows_ref, own_ref, scale_ref, out_ref):
    rows = rows_ref[...]
    far = jnp.dot(hi_ref[0], rows, preferred_element_type=jnp.float32)
    far = far + jnp.dot(lo_ref[0], rows, preferred_element_type=jnp.float32)
    out_ref[0] = (scale_ref[0] * own_ref[0].astype(jnp.float32) - far).astype(jnp.bfloat16)


def flux_chunk(table_hi, table_lo, rows, own, scale, chunk):
    q_count, slave_count, slots = table_hi.shape
    width = rows.shape[1] // q_count
    return pl.pallas_call(
        flux_kernel,
        grid=(q_count,),
        in_specs=[
            pl.BlockSpec((1, slave_count, slots), lambda q: (q, 0, 0)),
            pl.BlockSpec((1, slave_count, slots), lambda q: (q, 0, 0)),
            pl.BlockSpec((slots, width), lambda q: (0, q)),
            pl.BlockSpec((1, slave_count, width), lambda q: (q, 0, chunk)),
            pl.BlockSpec((1, slave_count, 1), lambda q: (q, 0, 0)),
        ],
        out_specs=pl.BlockSpec((1, slave_count, width), lambda q: (q, 0, 0)),
        out_shape=jax.ShapeDtypeStruct((q_count, slave_count, width), jnp.bfloat16),
    )(table_hi, table_lo, rows, own, scale)


def tile_kernel(tile_count, per_tile, source_ref, left_ref, flux_ref, out_ref):
    width = out_ref.shape[2]

    def body(x, carry):
        src = source_ref[x]

        @pl.when(src < tile_count)
        def _():
            first = pl.multiple_of(src * per_tile, per_tile)
            right = flux_ref[:, pl.ds(first, per_tile), :].reshape(-1, width)
            out_ref[x] = jnp.dot(
                left_ref[src], right, preferred_element_type=jnp.float32
            ).astype(jnp.bfloat16)

        @pl.when(src >= tile_count)
        def _():
            out_ref[x] = jnp.zeros(out_ref.shape[1:], out_ref.dtype)

        return carry

    lax.fori_loop(0, out_ref.shape[0], body, 0)


def packed_tiles_of(source, left, flux, per_tile):
    tile_slots = source.shape[0]
    tile_count, rows, depth = left.shape
    width = flux.shape[2]
    vmem = pltpu.MemorySpace.VMEM if hasattr(pltpu, "MemorySpace") else pltpu.TPUMemorySpace.VMEM
    return pl.pallas_call(
        functools.partial(tile_kernel, tile_count, per_tile),
        in_specs=[
            pl.BlockSpec(memory_space=pltpu.SMEM),
            pl.BlockSpec(memory_space=vmem),
            pl.BlockSpec(memory_space=vmem),
        ],
        out_specs=pl.BlockSpec(memory_space=vmem),
        out_shape=jax.ShapeDtypeStruct((tile_slots, rows, width), jnp.bfloat16),
    )(source, left, flux)


def assemble_kernel(rows_ref, tiles_ref, *refs):
    out_ref = refs[-1]
    out_ref[...] = jnp.zeros(out_ref.shape, out_ref.dtype)

    def body(x, carry):
        row = rows_ref[x]

        @pl.when(row >= 0)
        def _():
            out_ref[row] = out_ref[row] + tiles_ref[x].astype(jnp.float32)

        return carry

    lax.fori_loop(0, tiles_ref.shape[0], body, 0)


def assemble(rows, tiles, previous, chunk):
    tile_slots, depth, width = tiles.shape
    blocks = BR, depth, width
    specs = [
        pl.BlockSpec(memory_space=pltpu.SMEM),
        pl.BlockSpec(tiles.shape, lambda i: (0, 0, 0)),
    ]
    operands = [rows, tiles]
    aliases = {}
    if previous is not None:
        specs.append(pl.BlockSpec(memory_space=pl.ANY))
        operands.append(previous)
        aliases = {2: 0}
    return pl.pallas_call(
        assemble_kernel,
        grid=(1,),
        in_specs=specs,
        out_specs=pl.BlockSpec(blocks, lambda i: (0, 0, chunk)),
        out_shape=jax.ShapeDtypeStruct((BR, depth, width * SPLIT), jnp.float32),
        input_output_aliases=aliases,
    )(*operands)


def on_device(
    master_basis,
    master_weights,
    master_dest,
    master_slaves,
    slave_basis,
    slave_gain,
    tile_owner,
    tile_row,
):
    f32, bf16, i32 = jnp.float32, jnp.bfloat16, jnp.int32
    dom_count = lax.axis_size("dom")
    seg_count = master_basis.shape[0]
    capacity = 2 * seg_count // dom_count
    slots = dom_count * capacity
    slave_count = slave_basis.shape[0]
    tile_count = tile_row.shape[0]
    per_tile = slave_count // tile_count
    tile_capacity = max(2, 2 * tile_count // dom_count)
    tile_slots = dom_count * tile_capacity
    width = NP // SPLIT
    wcols = PAIRS * Q

    meta = jnp.concatenate(
        [
            master_weights.reshape(seg_count, wcols).astype(f32),
            master_dest.astype(f32),
            master_slaves.astype(f32) + 1.0,
        ],
        axis=1,
    )
    moved_meta = shifted(meta, "body", 1)
    moved_chunks = []
    for k in range(SPLIT):
        piece = master_basis[:, :, k * width:(k + 1) * width]
        if moved_chunks:
            piece, _ = lax.optimization_barrier((piece, moved_chunks[-1]))
        moved_chunks.append(shifted(piece, "body", 1))

    moved_dest = moved_meta[:, wcols].astype(i32)
    slot = slot_of(moved_dest, dom_count, capacity)
    placer = placer_of(slot, slots)
    records = jnp.concatenate([moved_meta[:, :wcols], moved_meta[:, wcols + 1:]], axis=1)
    packed_meta = jnp.dot(placer.astype(f32), records, precision=lax.Precision.HIGHEST)
    rec_cols = records.shape[1]

    tile_slot = slot_of(tile_owner[:, 0], dom_count, tile_capacity)
    tile_placer = placer_of(tile_slot, tile_slots)
    packed_rows = jnp.dot(tile_placer.astype(i32), tile_row + 1).astype(f32)

    send_meta = jnp.concatenate(
        [
            packed_meta.reshape(dom_count, capacity * rec_cols),
            packed_rows.reshape(dom_count, tile_capacity),
        ],
        axis=1,
    )
    got_meta = lax.all_to_all(send_meta, "dom", 0, 0, tiled=True)

    got_records = got_meta[:, : capacity * rec_cols].reshape(slots, rec_cols)
    got_weights = got_records[:, :wcols].reshape(slots, PAIRS, Q)
    got_owners = got_records[:, wcols:].astype(i32) - 1
    slave_ids = jnp.arange(slave_count, dtype=i32)
    table = None
    for p in range(PAIRS):
        term = jnp.where(
            got_owners[None, None, :, p] == slave_ids[None, :, None],
            jnp.transpose(got_weights[:, p, :])[:, None, :],
            0.0,
        )
        table = term if table is None else table + term
    table_hi = table.astype(bf16)
    table_lo = (table - table_hi.astype(f32)).astype(bf16)
    weight_sum = jnp.sum(table, axis=2)
    tables = lax.optimization_barrier((table_hi, table_lo, weight_sum))
    table_hi, table_lo, weight_sum = tables
    scale = (jnp.transpose(slave_gain[:, None]) + weight_sum)[:, :, None]

    got_rows = got_meta[:, capacity * rec_cols:].reshape(tile_slots).astype(i32) - 1
    tile_source = jnp.dot(tile_placer.astype(i32), jnp.arange(1, tile_count + 1, dtype=i32)) - 1
    tile_source = jnp.where(tile_source < 0, tile_count, tile_source)
    own = jnp.transpose(slave_basis, (1, 0, 2))
    left = jnp.transpose(
        slave_basis.reshape(tile_count, per_tile, Q, NP), (0, 3, 2, 1)
    ).reshape(tile_count, NP, Q * per_tile)

    staged = (tables, own, left, scale)
    got_chunks = []
    for k in range(SPLIT):
        moved = moved_chunks[k]
        if k == 1:
            moved, staged = lax.optimization_barrier((moved, staged))
            tables, own, left, scale = staged
            table_hi, table_lo, weight_sum = tables
        packed = jnp.dot(
            placer.astype(bf16),
            moved.reshape(seg_count, Q * width),
            preferred_element_type=f32,
        ).astype(bf16)
        got_chunks.append(
            lax.all_to_all(packed.reshape(dom_count, capacity, Q * width), "dom", 0, 0, tiled=True)
        )

    coupling = None
    for k in range(SPLIT):
        rows = got_chunks[k].reshape(slots, Q * width)
        flux = flux_chunk(table_hi, table_lo, rows, own, scale, k)
        packed_tiles = packed_tiles_of(tile_source, left, flux, per_tile)
        got_tiles = lax.all_to_all(
            packed_tiles.reshape(dom_count, tile_capacity * NP, width), "dom", 0, 0, tiled=True
        )
        coupling = assemble(got_rows, got_tiles.reshape(tile_slots, NP, width), coupling, k)
    return coupling


def solution(mesh):
    return jax.shard_map(
        on_device,
        mesh=mesh,
        in_specs=(
            P(("body", "dom"), None, None),
            P(("body", "dom"), None, None),
            P(("body", "dom"), None),
            P(("body", "dom"), None),
            P(("body", "dom"), None, None),
            P(("body", "dom")),
            P(("body", "dom"), None),
            P(("body", "dom")),
        ),
        out_specs=P(("body", "dom"), None, None),
        check_vma=False,
    )
```

```python
import functools

import jax
import jax.numpy as jnp
from jax import lax
from jax.experimental import pallas as pl
from jax.experimental.pallas import tpu as pltpu
from jax.sharding import PartitionSpec as P

NP = 256
Q = 16
PAIRS = 4
BR = 16
SPLIT = 2


def shifted(block, axis, distance):
    devices = range(lax.axis_size(axis))
    route = [((i - distance) % len(devices), i) for i in devices]
    return lax.ppermute(block, axis, route)


def slot_of(target, groups, capacity):
    onehot = (target[:, None] == jnp.arange(groups, dtype=jnp.int32)[None, :]).astype(jnp.int32)
    before = jnp.cumsum(onehot, axis=0) - onehot
    position = jnp.sum(before * onehot, axis=1)
    return target * capacity + position


def placer_of(slot, slots):
    return slot[None, :] == jnp.arange(slots, dtype=jnp.int32)[:, None]


def flux_kernel(hi_ref, lo_ref, rows_ref, own_ref, scale_ref, out_ref):
    rows = rows_ref[...]
    far = jnp.dot(hi_ref[0], rows, preferred_element_type=jnp.float32)
    far = far + jnp.dot(lo_ref[0], rows, preferred_element_type=jnp.float32)
    out_ref[0] = (scale_ref[0] * own_ref[0].astype(jnp.float32) - far).astype(jnp.bfloat16)


def flux_chunk(table_hi, table_lo, rows, own, scale, chunk):
    q_count, slave_count, slots = table_hi.shape
    width = rows.shape[1] // q_count
    return pl.pallas_call(
        flux_kernel,
        grid=(q_count,),
        in_specs=[
            pl.BlockSpec((1, slave_count, slots), lambda q: (q, 0, 0)),
            pl.BlockSpec((1, slave_count, slots), lambda q: (q, 0, 0)),
            pl.BlockSpec((slots, width), lambda q: (0, q)),
            pl.BlockSpec((1, slave_count, width), lambda q: (q, 0, chunk)),
            pl.BlockSpec((1, slave_count, 1), lambda q: (q, 0, 0)),
        ],
        out_specs=pl.BlockSpec((1, slave_count, width), lambda q: (q, 0, 0)),
        out_shape=jax.ShapeDtypeStruct((q_count, slave_count, width), jnp.bfloat16),
    )(table_hi, table_lo, rows, own, scale)


def tile_kernel(tile_count, per_tile, source_ref, left_ref, flux_ref, out_ref):
    width = out_ref.shape[2]

    def body(x, carry):
        src = source_ref[x]

        @pl.when(src < tile_count)
        def _():
            first = pl.multiple_of(src * per_tile, per_tile)
            right = flux_ref[:, pl.ds(first, per_tile), :].reshape(-1, width)
            out_ref[x] = jnp.dot(
                left_ref[src], right, preferred_element_type=jnp.float32
            ).astype(jnp.bfloat16)

        @pl.when(src >= tile_count)
        def _():
            out_ref[x] = jnp.zeros(out_ref.shape[1:], out_ref.dtype)

        return carry

    lax.fori_loop(0, out_ref.shape[0], body, 0)


def packed_tiles_of(source, left, flux, per_tile):
    tile_slots = source.shape[0]
    tile_count, rows, depth = left.shape
    width = flux.shape[2]
    vmem = pltpu.MemorySpace.VMEM if hasattr(pltpu, "MemorySpace") else pltpu.TPUMemorySpace.VMEM
    return pl.pallas_call(
        functools.partial(tile_kernel, tile_count, per_tile),
        in_specs=[
            pl.BlockSpec(memory_space=pltpu.SMEM),
            pl.BlockSpec(memory_space=vmem),
            pl.BlockSpec(memory_space=vmem),
        ],
        out_specs=pl.BlockSpec(memory_space=vmem),
        out_shape=jax.ShapeDtypeStruct((tile_slots, rows, width), jnp.bfloat16),
    )(source, left, flux)


def assemble_kernel(rows_ref, tiles_ref, *refs):
    out_ref = refs[-1]
    out_ref[...] = jnp.zeros(out_ref.shape, out_ref.dtype)

    def body(x, carry):
        row = rows_ref[x]

        @pl.when(row >= 0)
        def _():
            out_ref[row] = out_ref[row] + tiles_ref[x].astype(jnp.float32)

        return carry

    lax.fori_loop(0, tiles_ref.shape[0], body, 0)


def assemble(rows, tiles, previous, chunk):
    tile_slots, depth, width = tiles.shape
    blocks = BR, depth, width
    specs = [
        pl.BlockSpec(memory_space=pltpu.SMEM),
        pl.BlockSpec(tiles.shape, lambda i: (0, 0, 0)),
    ]
    operands = [rows, tiles]
    aliases = {}
    if previous is not None:
        specs.append(pl.BlockSpec(memory_space=pl.ANY))
        operands.append(previous)
        aliases = {2: 0}
    return pl.pallas_call(
        assemble_kernel,
        grid=(1,),
        in_specs=specs,
        out_specs=pl.BlockSpec(blocks, lambda i: (0, 0, chunk)),
        out_shape=jax.ShapeDtypeStruct((BR, depth, width * SPLIT), jnp.float32),
        input_output_aliases=aliases,
    )(*operands)


def on_device(
    master_basis,
    master_weights,
    master_dest,
    master_slaves,
    slave_basis,
    slave_gain,
    tile_owner,
    tile_row,
):
    f32, bf16, i32 = jnp.float32, jnp.bfloat16, jnp.int32
    dom_count = lax.axis_size("dom")
    seg_count = master_basis.shape[0]
    capacity = 2 * seg_count // dom_count
    slots = dom_count * capacity
    slave_count = slave_basis.shape[0]
    tile_count = tile_row.shape[0]
    per_tile = slave_count // tile_count
    tile_capacity = max(2, 2 * tile_count // dom_count)
    tile_slots = dom_count * tile_capacity
    width = NP // SPLIT
    wcols = PAIRS * Q

    meta = jnp.concatenate(
        [
            master_weights.reshape(seg_count, wcols).astype(f32),
            master_dest.astype(f32),
            master_slaves.astype(f32) + 1.0,
        ],
        axis=1,
    )
    moved_meta = shifted(meta, "body", 1)
    hops = lax.axis_size("body") - 1
    back_rows = seg_count * 3 // 16
    front_rows = seg_count - back_rows
    moved_chunks = []
    for k in range(SPLIT):
        piece = master_basis[:, :, k * width:(k + 1) * width]
        if moved_chunks:
            piece, _ = lax.optimization_barrier((piece, moved_chunks[-1]))
        front = shifted(piece[:front_rows], "body", 1)
        back = piece[front_rows:]
        for _ in range(hops):
            back = shifted(back, "body", -1)
        moved_chunks.append((front, back))

    moved_dest = moved_meta[:, wcols].astype(i32)
    slot = slot_of(moved_dest, dom_count, capacity)
    placer = placer_of(slot, slots)
    records = jnp.concatenate([moved_meta[:, :wcols], moved_meta[:, wcols + 1:]], axis=1)
    packed_meta = jnp.dot(placer.astype(f32), records, precision=lax.Precision.HIGHEST)
    rec_cols = records.shape[1]

    tile_slot = slot_of(tile_owner[:, 0], dom_count, tile_capacity)
    tile_placer = placer_of(tile_slot, tile_slots)
    packed_rows = jnp.dot(tile_placer.astype(i32), tile_row + 1).astype(f32)

    send_meta = jnp.concatenate(
        [
            packed_meta.reshape(dom_count, capacity * rec_cols),
            packed_rows.reshape(dom_count, tile_capacity),
        ],
        axis=1,
    )
    got_meta = lax.all_to_all(send_meta, "dom", 0, 0, tiled=True)

    got_records = got_meta[:, : capacity * rec_cols].reshape(slots, rec_cols)
    got_weights = got_records[:, :wcols].reshape(slots, PAIRS, Q)
    got_owners = got_records[:, wcols:].astype(i32) - 1
    slave_ids = jnp.arange(slave_count, dtype=i32)
    table = None
    for p in range(PAIRS):
        term = jnp.where(
            got_owners[None, None, :, p] == slave_ids[None, :, None],
            jnp.transpose(got_weights[:, p, :])[:, None, :],
            0.0,
        )
        table = term if table is None else table + term
    table_hi = table.astype(bf16)
    table_lo = (table - table_hi.astype(f32)).astype(bf16)
    weight_sum = jnp.sum(table, axis=2)
    tables = lax.optimization_barrier((table_hi, table_lo, weight_sum))
    table_hi, table_lo, weight_sum = tables
    scale = (jnp.transpose(slave_gain[:, None]) + weight_sum)[:, :, None]

    got_rows = got_meta[:, capacity * rec_cols:].reshape(tile_slots).astype(i32) - 1
    tile_source = jnp.dot(tile_placer.astype(i32), jnp.arange(1, tile_count + 1, dtype=i32)) - 1
    tile_source = jnp.where(tile_source < 0, tile_count, tile_source)
    own = jnp.transpose(slave_basis, (1, 0, 2))
    left = jnp.transpose(
        slave_basis.reshape(tile_count, per_tile, Q, NP), (0, 3, 2, 1)
    ).reshape(tile_count, NP, Q * per_tile)

    staged = (tables, own, left, scale)
    got_chunks = []
    for k in range(SPLIT):
        moved = moved_chunks[k]
        if k == 1:
            moved, staged = lax.optimization_barrier((moved, staged))
            tables, own, left, scale = staged
            table_hi, table_lo, weight_sum = tables
        front, back = moved
        packed = jnp.dot(
            placer[:, :front_rows].astype(bf16),
            front.reshape(front_rows, Q * width),
            preferred_element_type=f32,
        )
        packed = packed + jnp.dot(
            placer[:, front_rows:].astype(bf16),
            back.reshape(back_rows, Q * width),
            preferred_element_type=f32,
        )
        packed = packed.astype(bf16)
        got_chunks.append(
            lax.all_to_all(packed.reshape(dom_count, capacity, Q * width), "dom", 0, 0, tiled=True)
        )

    coupling = None
    for k in range(SPLIT):
        rows = got_chunks[k].reshape(slots, Q * width)
        flux = flux_chunk(table_hi, table_lo, rows, own, scale, k)
        packed_tiles = packed_tiles_of(tile_source, left, flux, per_tile)
        got_tiles = lax.all_to_all(
            packed_tiles.reshape(dom_count, tile_capacity * NP, width), "dom", 0, 0, tiled=True
        )
        coupling = assemble(got_rows, got_tiles.reshape(tile_slots, NP, width), coupling, k)
    return coupling


def solution(mesh):
    return jax.shard_map(
        on_device,
        mesh=mesh,
        in_specs=(
            P(("body", "dom"), None, None),
            P(("body", "dom"), None, None),
            P(("body", "dom"), None),
            P(("body", "dom"), None),
            P(("body", "dom"), None, None),
            P(("body", "dom")),
            P(("body", "dom"), None),
            P(("body", "dom")),
        ),
        out_specs=P(("body", "dom"), None, None),
        check_vma=False,
    )
```

```python
import functools

import jax
import jax.numpy as jnp
from jax import lax
from jax.experimental import pallas as pl
from jax.experimental.pallas import tpu as pltpu
from jax.sharding import PartitionSpec as P

NP = 256
Q = 16
PAIRS = 4
BR = 16
SPLIT = 2


def shifted(block, axis, distance):
    devices = range(lax.axis_size(axis))
    route = [((i - distance) % len(devices), i) for i in devices]
    return lax.ppermute(block, axis, route)


def slot_of(target, groups, capacity):
    onehot = (target[:, None] == jnp.arange(groups, dtype=jnp.int32)[None, :]).astype(jnp.int32)
    before = jnp.cumsum(onehot, axis=0) - onehot
    position = jnp.sum(before * onehot, axis=1)
    return target * capacity + position


def placer_of(slot, slots):
    return slot[None, :] == jnp.arange(slots, dtype=jnp.int32)[:, None]


def flux_kernel(hi_ref, lo_ref, rows_ref, own_ref, scale_ref, out_ref):
    rows = rows_ref[...]
    far = jnp.dot(hi_ref[0], rows, preferred_element_type=jnp.float32)
    far = far + jnp.dot(lo_ref[0], rows, preferred_element_type=jnp.float32)
    out_ref[0] = (scale_ref[0] * own_ref[0].astype(jnp.float32) - far).astype(jnp.bfloat16)


def flux_chunk(table_hi, table_lo, rows, own, scale, chunk):
    q_count, slave_count, slots = table_hi.shape
    width = rows.shape[1] // q_count
    return pl.pallas_call(
        flux_kernel,
        grid=(q_count,),
        in_specs=[
            pl.BlockSpec((1, slave_count, slots), lambda q: (q, 0, 0)),
            pl.BlockSpec((1, slave_count, slots), lambda q: (q, 0, 0)),
            pl.BlockSpec((slots, width), lambda q: (0, q)),
            pl.BlockSpec((1, slave_count, width), lambda q: (q, 0, chunk)),
            pl.BlockSpec((1, slave_count, 1), lambda q: (q, 0, 0)),
        ],
        out_specs=pl.BlockSpec((1, slave_count, width), lambda q: (q, 0, 0)),
        out_shape=jax.ShapeDtypeStruct((q_count, slave_count, width), jnp.bfloat16),
    )(table_hi, table_lo, rows, own, scale)


def tile_kernel(tile_count, per_tile, source_ref, left_ref, flux_ref, out_ref):
    width = out_ref.shape[2]

    def body(x, carry):
        src = source_ref[x]

        @pl.when(src < tile_count)
        def _():
            first = pl.multiple_of(src * per_tile, per_tile)
            right = flux_ref[:, pl.ds(first, per_tile), :].reshape(-1, width)
            out_ref[x] = jnp.dot(
                left_ref[src], right, preferred_element_type=jnp.float32
            ).astype(jnp.bfloat16)

        @pl.when(src >= tile_count)
        def _():
            out_ref[x] = jnp.zeros(out_ref.shape[1:], out_ref.dtype)

        return carry

    lax.fori_loop(0, out_ref.shape[0], body, 0)


def packed_tiles_of(source, left, flux, per_tile):
    tile_slots = source.shape[0]
    tile_count, rows, depth = left.shape
    width = flux.shape[2]
    vmem = pltpu.MemorySpace.VMEM if hasattr(pltpu, "MemorySpace") else pltpu.TPUMemorySpace.VMEM
    return pl.pallas_call(
        functools.partial(tile_kernel, tile_count, per_tile),
        in_specs=[
            pl.BlockSpec(memory_space=pltpu.SMEM),
            pl.BlockSpec(memory_space=vmem),
            pl.BlockSpec(memory_space=vmem),
        ],
        out_specs=pl.BlockSpec(memory_space=vmem),
        out_shape=jax.ShapeDtypeStruct((tile_slots, rows, width), jnp.bfloat16),
    )(source, left, flux)


def assemble_kernel(rows_ref, tiles_ref, *refs):
    out_ref = refs[-1]
    out_ref[...] = jnp.zeros(out_ref.shape, out_ref.dtype)

    def body(x, carry):
        row = rows_ref[x]

        @pl.when(row >= 0)
        def _():
            out_ref[row] = out_ref[row] + tiles_ref[x].astype(jnp.float32)

        return carry

    lax.fori_loop(0, tiles_ref.shape[0], body, 0)


def assemble(rows, tiles, previous, chunk):
    tile_slots, depth, width = tiles.shape
    blocks = BR, depth, width
    specs = [
        pl.BlockSpec(memory_space=pltpu.SMEM),
        pl.BlockSpec(tiles.shape, lambda i: (0, 0, 0)),
    ]
    operands = [rows, tiles]
    aliases = {}
    if previous is not None:
        specs.append(pl.BlockSpec(memory_space=pl.ANY))
        operands.append(previous)
        aliases = {2: 0}
    return pl.pallas_call(
        assemble_kernel,
        grid=(1,),
        in_specs=specs,
        out_specs=pl.BlockSpec(blocks, lambda i: (0, 0, chunk)),
        out_shape=jax.ShapeDtypeStruct((BR, depth, width * SPLIT), jnp.float32),
        input_output_aliases=aliases,
    )(*operands)


def on_device(
    master_basis,
    master_weights,
    master_dest,
    master_slaves,
    slave_basis,
    slave_gain,
    tile_owner,
    tile_row,
):
    f32, bf16, i32 = jnp.float32, jnp.bfloat16, jnp.int32
    dom_count = lax.axis_size("dom")
    seg_count = master_basis.shape[0]
    capacity = 2 * seg_count // dom_count
    slots = dom_count * capacity
    slave_count = slave_basis.shape[0]
    tile_count = tile_row.shape[0]
    per_tile = slave_count // tile_count
    tile_capacity = max(2, 2 * tile_count // dom_count)
    tile_slots = dom_count * tile_capacity
    width = NP // SPLIT
    wcols = PAIRS * Q

    meta = jnp.concatenate(
        [
            master_weights.reshape(seg_count, wcols).astype(f32),
            master_dest.astype(f32),
            master_slaves.astype(f32) + 1.0,
        ],
        axis=1,
    )
    moved_meta = shifted(meta, "body", 1)
    half = Q // 2
    pieces = []
    for k in range(SPLIT):
        piece = master_basis[:, :, k * width:(k + 1) * width]
        if k == 0:
            for h in range(2):
                part = piece[:, h * half:(h + 1) * half, :]
                pieces.append(part.reshape(seg_count // 2, Q, width))
        else:
            pieces.append(piece)
    moved_pieces = []
    for piece in pieces:
        if moved_pieces:
            piece, _ = lax.optimization_barrier((piece, moved_pieces[-1]))
        moved_pieces.append(shifted(piece, "body", 1))

    moved_dest = moved_meta[:, wcols].astype(i32)
    slot = slot_of(moved_dest, dom_count, capacity)
    placer = placer_of(slot, slots)
    records = jnp.concatenate([moved_meta[:, :wcols], moved_meta[:, wcols + 1:]], axis=1)
    packed_meta = jnp.dot(placer.astype(f32), records, precision=lax.Precision.HIGHEST)
    rec_cols = records.shape[1]

    tile_slot = slot_of(tile_owner[:, 0], dom_count, tile_capacity)
    tile_placer = placer_of(tile_slot, tile_slots)
    packed_rows = jnp.dot(tile_placer.astype(i32), tile_row + 1).astype(f32)

    send_meta = jnp.concatenate(
        [
            packed_meta.reshape(dom_count, capacity * rec_cols),
            packed_rows.reshape(dom_count, tile_capacity),
        ],
        axis=1,
    )
    got_meta = lax.all_to_all(send_meta, "dom", 0, 0, tiled=True)

    got_records = got_meta[:, : capacity * rec_cols].reshape(slots, rec_cols)
    got_weights = got_records[:, :wcols].reshape(slots, PAIRS, Q)
    got_owners = got_records[:, wcols:].astype(i32) - 1
    slave_ids = jnp.arange(slave_count, dtype=i32)
    table = None
    for p in range(PAIRS):
        term = jnp.where(
            got_owners[None, None, :, p] == slave_ids[None, :, None],
            jnp.transpose(got_weights[:, p, :])[:, None, :],
            0.0,
        )
        table = term if table is None else table + term
    table_hi = table.astype(bf16)
    table_lo = (table - table_hi.astype(f32)).astype(bf16)
    weight_sum = jnp.sum(table, axis=2)
    tables = lax.optimization_barrier((table_hi, table_lo, weight_sum))
    table_hi, table_lo, weight_sum = tables
    scale = (jnp.transpose(slave_gain[:, None]) + weight_sum)[:, :, None]

    got_rows = got_meta[:, capacity * rec_cols:].reshape(tile_slots).astype(i32) - 1
    tile_source = jnp.dot(tile_placer.astype(i32), jnp.arange(1, tile_count + 1, dtype=i32)) - 1
    tile_source = jnp.where(tile_source < 0, tile_count, tile_source)
    own = jnp.transpose(slave_basis, (1, 0, 2))
    left = jnp.transpose(
        slave_basis.reshape(tile_count, per_tile, Q, NP), (0, 3, 2, 1)
    ).reshape(tile_count, NP, Q * per_tile)

    staged = (tables, own, left, scale)
    got_pieces = []
    for j, moved in enumerate(moved_pieces):
        if j == len(moved_pieces) - 1:
            moved, staged = lax.optimization_barrier((moved, staged))
            tables, own, left, scale = staged
            table_hi, table_lo, weight_sum = tables
        cols = moved.size // seg_count
        packed = jnp.dot(
            placer.astype(bf16),
            moved.reshape(seg_count, cols),
            preferred_element_type=f32,
        ).astype(bf16)
        got = lax.all_to_all(packed.reshape(dom_count, capacity, cols), "dom", 0, 0, tiled=True)
        got_pieces.append(got.reshape(slots, cols))
    got_chunks = [jnp.concatenate(got_pieces[:2], axis=1), got_pieces[2]]

    coupling = None
    for k in range(SPLIT):
        rows = got_chunks[k].reshape(slots, Q * width)
        flux = flux_chunk(table_hi, table_lo, rows, own, scale, k)
        packed_tiles = packed_tiles_of(tile_source, left, flux, per_tile)
        got_tiles = lax.all_to_all(
            packed_tiles.reshape(dom_count, tile_capacity * NP, width), "dom", 0, 0, tiled=True
        )
        coupling = assemble(got_rows, got_tiles.reshape(tile_slots, NP, width), coupling, k)
    return coupling


def solution(mesh):
    return jax.shard_map(
        on_device,
        mesh=mesh,
        in_specs=(
            P(("body", "dom"), None, None),
            P(("body", "dom"), None, None),
            P(("body", "dom"), None),
            P(("body", "dom"), None),
            P(("body", "dom"), None, None),
            P(("body", "dom")),
            P(("body", "dom"), None),
            P(("body", "dom")),
        ),
        out_specs=P(("body", "dom"), None, None),
        check_vma=False,
    )
```

```python
import functools

import jax
import jax.numpy as jnp
from jax import lax
from jax.experimental import pallas as pl
from jax.experimental.pallas import tpu as pltpu
from jax.sharding import PartitionSpec as P

NP = 256
Q = 16
PAIRS = 4
BR = 16
SPLIT = 2


def shifted(block, axis, distance):
    devices = range(lax.axis_size(axis))
    route = [((i - distance) % len(devices), i) for i in devices]
    return lax.ppermute(block, axis, route)


def slot_of(target, groups, capacity):
    onehot = (target[:, None] == jnp.arange(groups, dtype=jnp.int32)[None, :]).astype(jnp.int32)
    before = jnp.cumsum(onehot, axis=0) - onehot
    position = jnp.sum(before * onehot, axis=1)
    return target * capacity + position


def placer_of(slot, slots):
    return slot[None, :] == jnp.arange(slots, dtype=jnp.int32)[:, None]


def flux_kernel(hi_ref, lo_ref, rows_ref, own_ref, scale_ref, out_ref):
    rows = rows_ref[...]
    far = jnp.dot(hi_ref[0], rows, preferred_element_type=jnp.float32)
    far = far + jnp.dot(lo_ref[0], rows, preferred_element_type=jnp.float32)
    out_ref[0] = (scale_ref[0] * own_ref[0].astype(jnp.float32) - far).astype(jnp.bfloat16)


def flux_chunk(table_hi, table_lo, rows, own, scale, chunk):
    q_count, slave_count, slots = table_hi.shape
    width = rows.shape[1] // q_count
    return pl.pallas_call(
        flux_kernel,
        grid=(q_count,),
        in_specs=[
            pl.BlockSpec((1, slave_count, slots), lambda q: (q, 0, 0)),
            pl.BlockSpec((1, slave_count, slots), lambda q: (q, 0, 0)),
            pl.BlockSpec((slots, width), lambda q: (0, q)),
            pl.BlockSpec((1, slave_count, width), lambda q: (q, 0, chunk)),
            pl.BlockSpec((1, slave_count, 1), lambda q: (q, 0, 0)),
        ],
        out_specs=pl.BlockSpec((1, slave_count, width), lambda q: (q, 0, 0)),
        out_shape=jax.ShapeDtypeStruct((q_count, slave_count, width), jnp.bfloat16),
    )(table_hi, table_lo, rows, own, scale)


def tile_kernel(tile_count, per_tile, source_ref, left_ref, flux_ref, out_ref):
    width = out_ref.shape[2]

    def body(x, carry):
        src = source_ref[x]

        @pl.when(src < tile_count)
        def _():
            first = pl.multiple_of(src * per_tile, per_tile)
            right = flux_ref[:, pl.ds(first, per_tile), :].reshape(-1, width)
            out_ref[x] = jnp.dot(
                left_ref[src], right, preferred_element_type=jnp.float32
            ).astype(jnp.bfloat16)

        @pl.when(src >= tile_count)
        def _():
            out_ref[x] = jnp.zeros(out_ref.shape[1:], out_ref.dtype)

        return carry

    lax.fori_loop(0, out_ref.shape[0], body, 0)


def packed_tiles_of(source, left, flux, per_tile):
    tile_slots = source.shape[0]
    tile_count, rows, depth = left.shape
    width = flux.shape[2]
    vmem = pltpu.MemorySpace.VMEM if hasattr(pltpu, "MemorySpace") else pltpu.TPUMemorySpace.VMEM
    return pl.pallas_call(
        functools.partial(tile_kernel, tile_count, per_tile),
        in_specs=[
            pl.BlockSpec(memory_space=pltpu.SMEM),
            pl.BlockSpec(memory_space=vmem),
            pl.BlockSpec(memory_space=vmem),
        ],
        out_specs=pl.BlockSpec(memory_space=vmem),
        out_shape=jax.ShapeDtypeStruct((tile_slots, rows, width), jnp.bfloat16),
    )(source, left, flux)


def assemble_kernel(rows_ref, tiles_ref, *refs):
    out_ref = refs[-1]
    out_ref[...] = jnp.zeros(out_ref.shape, out_ref.dtype)

    def body(x, carry):
        row = rows_ref[x]

        @pl.when(row >= 0)
        def _():
            out_ref[row] = out_ref[row] + tiles_ref[x].astype(jnp.float32)

        return carry

    lax.fori_loop(0, tiles_ref.shape[0], body, 0)


def assemble(rows, tiles, previous, chunk):
    tile_slots, depth, width = tiles.shape
    blocks = BR, depth, width
    specs = [
        pl.BlockSpec(memory_space=pltpu.SMEM),
        pl.BlockSpec(tiles.shape, lambda i: (0, 0, 0)),
    ]
    operands = [rows, tiles]
    aliases = {}
    if previous is not None:
        specs.append(pl.BlockSpec(memory_space=pl.ANY))
        operands.append(previous)
        aliases = {2: 0}
    return pl.pallas_call(
        assemble_kernel,
        grid=(1,),
        in_specs=specs,
        out_specs=pl.BlockSpec(blocks, lambda i: (0, 0, chunk)),
        out_shape=jax.ShapeDtypeStruct((BR, depth, width * SPLIT), jnp.float32),
        input_output_aliases=aliases,
    )(*operands)


def on_device(
    master_basis,
    master_weights,
    master_dest,
    master_slaves,
    slave_basis,
    slave_gain,
    tile_owner,
    tile_row,
):
    f32, bf16, i32 = jnp.float32, jnp.bfloat16, jnp.int32
    dom_count = lax.axis_size("dom")
    seg_count = master_basis.shape[0]
    capacity = 2 * seg_count // dom_count
    slots = dom_count * capacity
    slave_count = slave_basis.shape[0]
    tile_count = tile_row.shape[0]
    per_tile = slave_count // tile_count
    tile_capacity = max(2, 2 * tile_count // dom_count)
    tile_slots = dom_count * tile_capacity
    width = NP // SPLIT
    wcols = PAIRS * Q

    meta = jnp.concatenate(
        [
            master_weights.reshape(seg_count, wcols).astype(f32),
            master_dest.astype(f32),
            master_slaves.astype(f32) + 1.0,
        ],
        axis=1,
    )
    moved_meta = shifted(meta, "body", 1)
    half = Q // 2
    pieces = []
    for k in range(SPLIT):
        piece = master_basis[:, :, k * width:(k + 1) * width]
        if k == 0:
            for h in range(2):
                part = piece[:, h * half:(h + 1) * half, :]
                pieces.append(part.reshape(seg_count // 2, Q, width))
        else:
            pieces.append(piece)
    own = jnp.transpose(slave_basis, (1, 0, 2))
    left = jnp.transpose(
        slave_basis.reshape(tile_count, per_tile, Q, NP), (0, 3, 2, 1)
    ).reshape(tile_count, NP, Q * per_tile)
    moved_pieces = []
    for j in range(len(pieces)):
        piece = pieces[j]
        if j == 1:
            piece, moved_pieces[-1], early = lax.optimization_barrier(
                (piece, moved_pieces[-1], (own, left, pieces[2]))
            )
            own, left, pieces[2] = early
        elif moved_pieces:
            piece, moved_pieces[-1] = lax.optimization_barrier((piece, moved_pieces[-1]))
        moved_pieces.append(shifted(piece, "body", 1))

    moved_dest = moved_meta[:, wcols].astype(i32)
    slot = slot_of(moved_dest, dom_count, capacity)
    placer = placer_of(slot, slots)
    records = jnp.concatenate([moved_meta[:, :wcols], moved_meta[:, wcols + 1:]], axis=1)
    packed_meta = jnp.dot(placer.astype(f32), records, precision=lax.Precision.HIGHEST)
    rec_cols = records.shape[1]

    tile_slot = slot_of(tile_owner[:, 0], dom_count, tile_capacity)
    tile_placer = placer_of(tile_slot, tile_slots)
    packed_rows = jnp.dot(tile_placer.astype(i32), tile_row + 1).astype(f32)

    send_meta = jnp.concatenate(
        [
            packed_meta.reshape(dom_count, capacity * rec_cols),
            packed_rows.reshape(dom_count, tile_capacity),
        ],
        axis=1,
    )
    got_meta = lax.all_to_all(send_meta, "dom", 0, 0, tiled=True)

    got_records = got_meta[:, : capacity * rec_cols].reshape(slots, rec_cols)
    got_weights = got_records[:, :wcols].reshape(slots, PAIRS, Q)
    got_owners = got_records[:, wcols:].astype(i32) - 1
    slave_ids = jnp.arange(slave_count, dtype=i32)
    table = None
    for p in range(PAIRS):
        term = jnp.where(
            got_owners[None, None, :, p] == slave_ids[None, :, None],
            jnp.transpose(got_weights[:, p, :])[:, None, :],
            0.0,
        )
        table = term if table is None else table + term
    table_hi = table.astype(bf16)
    table_lo = (table - table_hi.astype(f32)).astype(bf16)
    weight_sum = jnp.sum(table, axis=2)
    tables = lax.optimization_barrier((table_hi, table_lo, weight_sum))
    table_hi, table_lo, weight_sum = tables
    scale = (jnp.transpose(slave_gain[:, None]) + weight_sum)[:, :, None]

    got_rows = got_meta[:, capacity * rec_cols:].reshape(tile_slots).astype(i32) - 1
    tile_source = jnp.dot(tile_placer.astype(i32), jnp.arange(1, tile_count + 1, dtype=i32)) - 1
    tile_source = jnp.where(tile_source < 0, tile_count, tile_source)

    staged = (tables, own, left, scale)
    got_pieces = []
    for j, moved in enumerate(moved_pieces):
        if j == len(moved_pieces) - 1:
            moved, staged = lax.optimization_barrier((moved, staged))
            tables, own, left, scale = staged
            table_hi, table_lo, weight_sum = tables
        cols = moved.size // seg_count
        packed = jnp.dot(
            placer.astype(bf16),
            moved.reshape(seg_count, cols),
            preferred_element_type=f32,
        ).astype(bf16)
        got = lax.all_to_all(packed.reshape(dom_count, capacity, cols), "dom", 0, 0, tiled=True)
        got_pieces.append(got.reshape(slots, cols))
    got_chunks = [jnp.concatenate(got_pieces[:2], axis=1), got_pieces[2]]

    coupling = None
    for k in range(SPLIT):
        rows = got_chunks[k].reshape(slots, Q * width)
        flux = flux_chunk(table_hi, table_lo, rows, own, scale, k)
        packed_tiles = packed_tiles_of(tile_source, left, flux, per_tile)
        got_tiles = lax.all_to_all(
            packed_tiles.reshape(dom_count, tile_capacity * NP, width), "dom", 0, 0, tiled=True
        )
        coupling = assemble(got_rows, got_tiles.reshape(tile_slots, NP, width), coupling, k)
    return coupling


def solution(mesh):
    return jax.shard_map(
        on_device,
        mesh=mesh,
        in_specs=(
            P(("body", "dom"), None, None),
            P(("body", "dom"), None, None),
            P(("body", "dom"), None),
            P(("body", "dom"), None),
            P(("body", "dom"), None, None),
            P(("body", "dom")),
            P(("body", "dom"), None),
            P(("body", "dom")),
        ),
        out_specs=P(("body", "dom"), None, None),
        check_vma=False,
    )
```

```python
import functools

import jax
import jax.numpy as jnp
from jax import lax
from jax.experimental import pallas as pl
from jax.experimental.pallas import tpu as pltpu
from jax.sharding import PartitionSpec as P

NP = 256
Q = 16
PAIRS = 4
BR = 16
SPLIT = 2


def shifted(block, axis, distance):
    devices = range(lax.axis_size(axis))
    route = [((i - distance) % len(devices), i) for i in devices]
    return lax.ppermute(block, axis, route)


def slot_of(target, groups, capacity):
    onehot = (target[:, None] == jnp.arange(groups, dtype=jnp.int32)[None, :]).astype(jnp.int32)
    before = jnp.cumsum(onehot, axis=0) - onehot
    position = jnp.sum(before * onehot, axis=1)
    return target * capacity + position


def placer_of(slot, slots):
    return slot[None, :] == jnp.arange(slots, dtype=jnp.int32)[:, None]


def flux_kernel(hi_ref, lo_ref, rows_ref, own_ref, scale_ref, out_ref):
    rows = rows_ref[...]
    far = jnp.dot(hi_ref[0], rows, preferred_element_type=jnp.float32)
    far = far + jnp.dot(lo_ref[0], rows, preferred_element_type=jnp.float32)
    out_ref[0] = (scale_ref[0] * own_ref[0].astype(jnp.float32) - far).astype(jnp.bfloat16)


def flux_chunk(table_hi, table_lo, rows, own, scale, chunk):
    q_count, slave_count, slots = table_hi.shape
    width = rows.shape[1] // q_count
    return pl.pallas_call(
        flux_kernel,
        grid=(q_count,),
        in_specs=[
            pl.BlockSpec((1, slave_count, slots), lambda q: (q, 0, 0)),
            pl.BlockSpec((1, slave_count, slots), lambda q: (q, 0, 0)),
            pl.BlockSpec((slots, width), lambda q: (0, q)),
            pl.BlockSpec((1, slave_count, width), lambda q: (q, 0, chunk)),
            pl.BlockSpec((1, slave_count, 1), lambda q: (q, 0, 0)),
        ],
        out_specs=pl.BlockSpec((1, slave_count, width), lambda q: (q, 0, 0)),
        out_shape=jax.ShapeDtypeStruct((q_count, slave_count, width), jnp.bfloat16),
    )(table_hi, table_lo, rows, own, scale)


def tile_kernel(tile_count, per_tile, source_ref, left_ref, flux_ref, out_ref):
    width = out_ref.shape[2]

    def body(x, carry):
        src = source_ref[x]

        @pl.when(src < tile_count)
        def _():
            first = pl.multiple_of(src * per_tile, per_tile)
            right = flux_ref[:, pl.ds(first, per_tile), :].reshape(-1, width)
            out_ref[x] = jnp.dot(
                left_ref[src], right, preferred_element_type=jnp.float32
            ).astype(jnp.bfloat16)

        @pl.when(src >= tile_count)
        def _():
            out_ref[x] = jnp.zeros(out_ref.shape[1:], out_ref.dtype)

        return carry

    lax.fori_loop(0, out_ref.shape[0], body, 0)


def packed_tiles_of(source, left, flux, per_tile):
    tile_slots = source.shape[0]
    tile_count, rows, depth = left.shape
    width = flux.shape[2]
    vmem = pltpu.MemorySpace.VMEM if hasattr(pltpu, "MemorySpace") else pltpu.TPUMemorySpace.VMEM
    return pl.pallas_call(
        functools.partial(tile_kernel, tile_count, per_tile),
        in_specs=[
            pl.BlockSpec(memory_space=pltpu.SMEM),
            pl.BlockSpec(memory_space=vmem),
            pl.BlockSpec(memory_space=vmem),
        ],
        out_specs=pl.BlockSpec(memory_space=vmem),
        out_shape=jax.ShapeDtypeStruct((tile_slots, rows, width), jnp.bfloat16),
    )(source, left, flux)


def assemble_kernel(rows_ref, tiles_ref, *refs):
    out_ref = refs[-1]
    out_ref[...] = jnp.zeros(out_ref.shape, out_ref.dtype)

    def body(x, carry):
        row = rows_ref[x]

        @pl.when(row >= 0)
        def _():
            out_ref[row] = out_ref[row] + tiles_ref[x].astype(jnp.float32)

        return carry

    lax.fori_loop(0, tiles_ref.shape[0], body, 0)


def assemble(rows, tiles, previous, chunk):
    tile_slots, depth, width = tiles.shape
    steps = 4
    band = depth // steps
    blocks = BR, band, width
    specs = [
        pl.BlockSpec(memory_space=pltpu.SMEM),
        pl.BlockSpec((tile_slots, band, width), lambda i: (0, i, 0)),
    ]
    operands = [rows, tiles]
    aliases = {}
    if previous is not None:
        specs.append(pl.BlockSpec(memory_space=pl.ANY))
        operands.append(previous)
        aliases = {2: 0}
    return pl.pallas_call(
        assemble_kernel,
        grid=(steps,),
        in_specs=specs,
        out_specs=pl.BlockSpec(blocks, lambda i: (0, i, chunk)),
        out_shape=jax.ShapeDtypeStruct((BR, depth, width * SPLIT), jnp.float32),
        input_output_aliases=aliases,
    )(*operands)


def on_device(
    master_basis,
    master_weights,
    master_dest,
    master_slaves,
    slave_basis,
    slave_gain,
    tile_owner,
    tile_row,
):
    f32, bf16, i32 = jnp.float32, jnp.bfloat16, jnp.int32
    dom_count = lax.axis_size("dom")
    seg_count = master_basis.shape[0]
    capacity = 2 * seg_count // dom_count
    slots = dom_count * capacity
    slave_count = slave_basis.shape[0]
    tile_count = tile_row.shape[0]
    per_tile = slave_count // tile_count
    tile_capacity = max(2, 2 * tile_count // dom_count)
    tile_slots = dom_count * tile_capacity
    width = NP // SPLIT
    wcols = PAIRS * Q

    meta = jnp.concatenate(
        [
            master_weights.reshape(seg_count, wcols).astype(f32),
            master_dest.astype(f32),
            master_slaves.astype(f32) + 1.0,
        ],
        axis=1,
    )
    moved_meta = shifted(meta, "body", 1)
    moved_chunks = []
    for k in range(SPLIT):
        piece = master_basis[:, :, k * width:(k + 1) * width]
        if moved_chunks:
            piece, _ = lax.optimization_barrier((piece, moved_chunks[-1]))
        moved_chunks.append(shifted(piece, "body", 1))

    moved_dest = moved_meta[:, wcols].astype(i32)
    slot = slot_of(moved_dest, dom_count, capacity)
    placer = placer_of(slot, slots)
    select = lax.optimization_barrier(placer.astype(bf16))
    records = jnp.concatenate([moved_meta[:, :wcols], moved_meta[:, wcols + 1:]], axis=1)
    packed_meta = jnp.dot(placer.astype(f32), records, precision=lax.Precision.HIGHEST)
    rec_cols = records.shape[1]

    tile_slot = slot_of(tile_owner[:, 0], dom_count, tile_capacity)
    tile_placer = placer_of(tile_slot, tile_slots)
    packed_rows = jnp.dot(tile_placer.astype(i32), tile_row + 1).astype(f32)

    send_meta = jnp.concatenate(
        [
            packed_meta.reshape(dom_count, capacity * rec_cols),
            packed_rows.reshape(dom_count, tile_capacity),
        ],
        axis=1,
    )
    got_meta = lax.all_to_all(send_meta, "dom", 0, 0, tiled=True)

    got_records = got_meta[:, : capacity * rec_cols].reshape(slots, rec_cols)
    got_weights = got_records[:, :wcols].reshape(slots, PAIRS, Q)
    got_owners = got_records[:, wcols:].astype(i32) - 1
    slave_ids = jnp.arange(slave_count, dtype=i32)
    table = None
    for p in range(PAIRS):
        term = jnp.where(
            got_owners[None, None, :, p] == slave_ids[None, :, None],
            jnp.transpose(got_weights[:, p, :])[:, None, :],
            0.0,
        )
        table = term if table is None else table + term
    table_hi = table.astype(bf16)
    table_lo = (table - table_hi.astype(f32)).astype(bf16)
    weight_sum = jnp.sum(table, axis=2)
    tables = lax.optimization_barrier((table_hi, table_lo, weight_sum))
    table_hi, table_lo, weight_sum = tables
    scale = (jnp.transpose(slave_gain[:, None]) + weight_sum)[:, :, None]

    got_rows = got_meta[:, capacity * rec_cols:].reshape(tile_slots).astype(i32) - 1
    tile_source = jnp.dot(tile_placer.astype(i32), jnp.arange(1, tile_count + 1, dtype=i32)) - 1
    tile_source = jnp.where(tile_source < 0, tile_count, tile_source)
    own = jnp.transpose(slave_basis, (1, 0, 2))
    left = jnp.transpose(
        slave_basis.reshape(tile_count, per_tile, Q, NP), (0, 3, 2, 1)
    ).reshape(tile_count, NP, Q * per_tile)

    staged = (tables, own, left, scale)
    got_chunks = []
    for k in range(SPLIT):
        moved = moved_chunks[k]
        if k == 1:
            moved, staged = lax.optimization_barrier((moved, staged))
            tables, own, left, scale = staged
            table_hi, table_lo, weight_sum = tables
        packed = jnp.dot(
            select,
            moved.reshape(seg_count, Q * width),
            preferred_element_type=f32,
        ).astype(bf16)
        got_chunks.append(
            lax.all_to_all(packed.reshape(dom_count, capacity, Q * width), "dom", 0, 0, tiled=True)
        )

    coupling = None
    for k in range(SPLIT):
        rows = got_chunks[k].reshape(slots, Q * width)
        flux = flux_chunk(table_hi, table_lo, rows, own, scale, k)
        packed_tiles = packed_tiles_of(tile_source, left, flux, per_tile)
        got_tiles = lax.all_to_all(
            packed_tiles.reshape(dom_count, tile_capacity * NP, width), "dom", 0, 0, tiled=True
        )
        coupling = assemble(got_rows, got_tiles.reshape(tile_slots, NP, width), coupling, k)
    return coupling


def solution(mesh):
    return jax.shard_map(
        on_device,
        mesh=mesh,
        in_specs=(
            P(("body", "dom"), None, None),
            P(("body", "dom"), None, None),
            P(("body", "dom"), None),
            P(("body", "dom"), None),
            P(("body", "dom"), None, None),
            P(("body", "dom")),
            P(("body", "dom"), None),
            P(("body", "dom")),
        ),
        out_specs=P(("body", "dom"), None, None),
        check_vma=False,
    )
```

```python
import functools

import jax
import jax.numpy as jnp
from jax import lax
from jax.experimental import pallas as pl
from jax.experimental.pallas import tpu as pltpu
from jax.sharding import PartitionSpec as P

NP = 256
Q = 16
PAIRS = 4
BR = 16
SPLIT = 2


def shifted(block, axis, distance):
    devices = range(lax.axis_size(axis))
    route = [((i - distance) % len(devices), i) for i in devices]
    return lax.ppermute(block, axis, route)


def slot_of(target, groups, capacity):
    onehot = (target[:, None] == jnp.arange(groups, dtype=jnp.int32)[None, :]).astype(jnp.int32)
    before = jnp.cumsum(onehot, axis=0) - onehot
    position = jnp.sum(before * onehot, axis=1)
    return target * capacity + position


def placer_of(slot, slots):
    return slot[None, :] == jnp.arange(slots, dtype=jnp.int32)[:, None]


def flux_kernel(hi_ref, lo_ref, rows_ref, own_ref, scale_ref, out_ref):
    rows = rows_ref[...]
    far = jnp.dot(hi_ref[0], rows, preferred_element_type=jnp.float32)
    far = far + jnp.dot(lo_ref[0], rows, preferred_element_type=jnp.float32)
    out_ref[0] = (scale_ref[0] * own_ref[0].astype(jnp.float32) - far).astype(jnp.bfloat16)


def flux_chunk(table_hi, table_lo, rows, own, scale, chunk):
    q_count, slave_count, slots = table_hi.shape
    width = rows.shape[1] // q_count
    return pl.pallas_call(
        flux_kernel,
        grid=(q_count,),
        in_specs=[
            pl.BlockSpec((1, slave_count, slots), lambda q: (q, 0, 0)),
            pl.BlockSpec((1, slave_count, slots), lambda q: (q, 0, 0)),
            pl.BlockSpec((slots, width), lambda q: (0, q)),
            pl.BlockSpec((1, slave_count, width), lambda q: (q, 0, chunk)),
            pl.BlockSpec((1, slave_count, 1), lambda q: (q, 0, 0)),
        ],
        out_specs=pl.BlockSpec((1, slave_count, width), lambda q: (q, 0, 0)),
        out_shape=jax.ShapeDtypeStruct((q_count, slave_count, width), jnp.bfloat16),
    )(table_hi, table_lo, rows, own, scale)


def tile_kernel(tile_count, per_tile, source_ref, left_ref, flux_ref, out_ref):
    width = out_ref.shape[2]

    def body(x, carry):
        src = source_ref[x]

        @pl.when(src < tile_count)
        def _():
            first = pl.multiple_of(src * per_tile, per_tile)
            right = flux_ref[:, pl.ds(first, per_tile), :].reshape(-1, width)
            out_ref[x] = jnp.dot(
                left_ref[src], right, preferred_element_type=jnp.float32
            ).astype(jnp.bfloat16)

        @pl.when(src >= tile_count)
        def _():
            out_ref[x] = jnp.zeros(out_ref.shape[1:], out_ref.dtype)

        return carry

    lax.fori_loop(0, out_ref.shape[0], body, 0)


def packed_tiles_of(source, left, flux, per_tile):
    tile_slots = source.shape[0]
    tile_count, rows, depth = left.shape
    width = flux.shape[2]
    vmem = pltpu.MemorySpace.VMEM if hasattr(pltpu, "MemorySpace") else pltpu.TPUMemorySpace.VMEM
    return pl.pallas_call(
        functools.partial(tile_kernel, tile_count, per_tile),
        in_specs=[
            pl.BlockSpec(memory_space=pltpu.SMEM),
            pl.BlockSpec(memory_space=vmem),
            pl.BlockSpec(memory_space=vmem),
        ],
        out_specs=pl.BlockSpec(memory_space=vmem),
        out_shape=jax.ShapeDtypeStruct((tile_slots, rows, width), jnp.bfloat16),
    )(source, left, flux)


def assemble_kernel(rows_ref, tiles_ref, *refs):
    out_ref = refs[-1]
    out_ref[...] = jnp.zeros(out_ref.shape, out_ref.dtype)

    def body(x, carry):
        row = rows_ref[x]

        @pl.when(row >= 0)
        def _():
            out_ref[row] = out_ref[row] + tiles_ref[x].astype(jnp.float32)

        return carry

    lax.fori_loop(0, tiles_ref.shape[0], body, 0)


def assemble(rows, tiles, previous, chunk):
    tile_slots, depth, width = tiles.shape
    blocks = BR, depth, width
    specs = [
        pl.BlockSpec(memory_space=pltpu.SMEM),
        pl.BlockSpec(tiles.shape, lambda i: (0, 0, 0)),
    ]
    operands = [rows, tiles]
    aliases = {}
    if previous is not None:
        specs.append(pl.BlockSpec(memory_space=pl.ANY))
        operands.append(previous)
        aliases = {2: 0}
    return pl.pallas_call(
        assemble_kernel,
        grid=(1,),
        in_specs=specs,
        out_specs=pl.BlockSpec(blocks, lambda i: (0, 0, chunk)),
        out_shape=jax.ShapeDtypeStruct((BR, depth, width * SPLIT), jnp.float32),
        input_output_aliases=aliases,
    )(*operands)


def on_device(
    master_basis,
    master_weights,
    master_dest,
    master_slaves,
    slave_basis,
    slave_gain,
    tile_owner,
    tile_row,
):
    f32, bf16, i32 = jnp.float32, jnp.bfloat16, jnp.int32
    dom_count = lax.axis_size("dom")
    seg_count = master_basis.shape[0]
    capacity = 2 * seg_count // dom_count
    slots = dom_count * capacity
    slave_count = slave_basis.shape[0]
    tile_count = tile_row.shape[0]
    per_tile = slave_count // tile_count
    tile_capacity = max(2, 2 * tile_count // dom_count)
    tile_slots = dom_count * tile_capacity
    width = NP // SPLIT
    wcols = PAIRS * Q

    meta = jnp.concatenate(
        [
            master_weights.reshape(seg_count, wcols).astype(f32),
            master_dest.astype(f32),
            master_slaves.astype(f32) + 1.0,
        ],
        axis=1,
    )
    moved_chunks = []
    for k in range(SPLIT):
        piece = master_basis[:, :, k * width:(k + 1) * width]
        if moved_chunks:
            piece, _ = lax.optimization_barrier((piece, moved_chunks[-1]))
        else:
            piece, meta = lax.optimization_barrier((piece, meta))
            moved_meta = shifted(meta, "body", 1)
        moved_chunks.append(shifted(piece, "body", 1))

    moved_dest = moved_meta[:, wcols].astype(i32)
    slot = slot_of(moved_dest, dom_count, capacity)
    placer = placer_of(slot, slots)
    records = jnp.concatenate([moved_meta[:, :wcols], moved_meta[:, wcols + 1:]], axis=1)
    packed_meta = jnp.dot(placer.astype(f32), records, precision=lax.Precision.HIGHEST)
    rec_cols = records.shape[1]

    tile_slot = slot_of(tile_owner[:, 0], dom_count, tile_capacity)
    tile_placer = placer_of(tile_slot, tile_slots)
    packed_rows = jnp.dot(tile_placer.astype(i32), tile_row + 1).astype(f32)

    send_meta = jnp.concatenate(
        [
            packed_meta.reshape(dom_count, capacity * rec_cols),
            packed_rows.reshape(dom_count, tile_capacity),
        ],
        axis=1,
    )
    got_meta = lax.all_to_all(send_meta, "dom", 0, 0, tiled=True)

    got_records = got_meta[:, : capacity * rec_cols].reshape(slots, rec_cols)
    got_weights = got_records[:, :wcols].reshape(slots, PAIRS, Q)
    got_owners = got_records[:, wcols:].astype(i32) - 1
    slave_ids = jnp.arange(slave_count, dtype=i32)
    table = None
    for p in range(PAIRS):
        term = jnp.where(
            got_owners[None, None, :, p] == slave_ids[None, :, None],
            jnp.transpose(got_weights[:, p, :])[:, None, :],
            0.0,
        )
        table = term if table is None else table + term
    table_hi = table.astype(bf16)
    table_lo = (table - table_hi.astype(f32)).astype(bf16)
    weight_sum = jnp.sum(table, axis=2)
    tables = lax.optimization_barrier((table_hi, table_lo, weight_sum))
    table_hi, table_lo, weight_sum = tables
    scale = (jnp.transpose(slave_gain[:, None]) + weight_sum)[:, :, None]

    got_rows = got_meta[:, capacity * rec_cols:].reshape(tile_slots).astype(i32) - 1
    tile_source = jnp.dot(tile_placer.astype(i32), jnp.arange(1, tile_count + 1, dtype=i32)) - 1
    tile_source = jnp.where(tile_source < 0, tile_count, tile_source)
    own = jnp.transpose(slave_basis, (1, 0, 2))
    left = jnp.transpose(
        slave_basis.reshape(tile_count, per_tile, Q, NP), (0, 3, 2, 1)
    ).reshape(tile_count, NP, Q * per_tile)

    staged = (tables, own, left, scale)
    got_chunks = []
    for k in range(SPLIT):
        moved = moved_chunks[k]
        if k == 1:
            moved, staged = lax.optimization_barrier((moved, staged))
            tables, own, left, scale = staged
            table_hi, table_lo, weight_sum = tables
        packed = jnp.dot(
            placer.astype(bf16),
            moved.reshape(seg_count, Q * width),
            preferred_element_type=f32,
        ).astype(bf16)
        got_chunks.append(
            lax.all_to_all(packed.reshape(dom_count, capacity, Q * width), "dom", 0, 0, tiled=True)
        )

    coupling = None
    for k in range(SPLIT):
        rows = got_chunks[k].reshape(slots, Q * width)
        flux = flux_chunk(table_hi, table_lo, rows, own, scale, k)
        packed_tiles = packed_tiles_of(tile_source, left, flux, per_tile)
        got_tiles = lax.all_to_all(
            packed_tiles.reshape(dom_count, tile_capacity * NP, width), "dom", 0, 0, tiled=True
        )
        coupling = assemble(got_rows, got_tiles.reshape(tile_slots, NP, width), coupling, k)
    return coupling


def solution(mesh):
    return jax.shard_map(
        on_device,
        mesh=mesh,
        in_specs=(
            P(("body", "dom"), None, None),
            P(("body", "dom"), None, None),
            P(("body", "dom"), None),
            P(("body", "dom"), None),
            P(("body", "dom"), None, None),
            P(("body", "dom")),
            P(("body", "dom"), None),
            P(("body", "dom")),
        ),
        out_specs=P(("body", "dom"), None, None),
        check_vma=False,
    )
```
